256 devices in a mesh: dp: 8 (over z_lo, x), expert: 32 (over z_hi, y, core).
Axes of the slice: x: 4, y: 4, z: 8 (z_hi: 4, z_lo: 2; z = z_hi * 2 + z_lo), core: 2. Of those that a mesh axis runs over, the one named last changes fastest.
Arguments:
- tokens: bfloat16 [8192, 4096], P('expert', 'dp'), may hold values from -6 to 6
- out_grad: bfloat16 [8192, 4096], P('expert', 'dp'), may hold values from -3 to 3
- expert_ids: int32 [8192, 2], P('expert'), may hold values from 0 to 31, as said below
- gate_probs: float32 [8192, 2], P('expert'), may hold values from 0.25 to 1
- w_gate: bfloat16 [32, 4096, 1024], P('expert', 'dp'), may hold values from -0.09375 to 0.09375
- w_up: bfloat16 [32, 4096, 1024], P('expert', 'dp'), may hold values from -0.09375 to 0.09375
- w_down: bfloat16 [32, 1024, 4096], P('expert', None, 'dp'), may hold values from -0.1875 to 0.1875
Outputs:
- token_grad: bfloat16 [8192, 4096], P('expert', 'dp')
- grad_w_gate: float32 [32, 4096, 1024], P('expert', 'dp')
- grad_w_up: float32 [32, 4096, 1024], P('expert', 'dp')
- grad_w_down: float32 [32, 1024, 4096], P('expert', None, 'dp')
The draws below stay inside these ranges and needn't reach their ends.
Inputs may be any that keep to these rules, and one draw needn't show every extreme that they name: `expert_ids`: A token's two ids differ. Among the tokens of one aligned block of 256 tokens no expert is named more than 32 times; 4 experts, the same for every block, are named exactly 32 times in each block.
All inputs are finite; a program needn't handle non-finite values.
Results may differ from the reference program's by a relative error of at most 0.02.
Values may be sent and summed in bfloat16 or wider, within the bound.
No kernel may reach another device: no remote copies, remote signals or barrier semaphores. Data moves between devices by JAX's collectives and lax.ppermute only.
A program may use at most 64 MiB of HBM per device.

```python
import jax
import jax.numpy as jnp
from jax import lax

D = 4096
FF = 1024
TOK_DEV = 256
HOT = 4
MOST = 32
EXPERTS = 32
TOKENS = 8192
N_DP = 8
N_EXPERT = 32


def draw_expert_ids(key, part):
    blocks = TOKENS // TOK_DEV
    pick_count = 2 * TOK_DEV
    total_slots = EXPERTS * MOST
    expert_order = jax.random.permutation(jax.random.fold_in(key, 11), EXPERTS)
    expert_place = jnp.argsort(expert_order)
    is_hot = expert_place < HOT
    slot_expert = jnp.repeat(jnp.arange(EXPERTS, dtype=jnp.int32), MOST)
    slot_hot = is_hot[slot_expert]

    def one_block(block_key):
        shuffle = jax.random.permutation(jax.random.fold_in(block_key, 1), total_slots).astype(jnp.int32)
        slot_score = jnp.where(slot_hot, -1 - jnp.arange(total_slots, dtype=jnp.int32), shuffle)
        chosen = jnp.argsort(slot_score)[:pick_count]
        named_sorted = jnp.sort(slot_expert[chosen])
        paired = jnp.stack([named_sorted[:TOK_DEV], named_sorted[TOK_DEV:]], axis=1)
        paired = paired[jax.random.permutation(jax.random.fold_in(block_key, 2), TOK_DEV)]
        flip_pair = jax.random.randint(jax.random.fold_in(block_key, 3), (TOK_DEV, 1), 0, 2)
        return jnp.where(flip_pair == 1, paired[:, ::-1], paired)
    block_keys = jax.random.split(jax.random.fold_in(key, 12), blocks)
    return jax.vmap(one_block)(block_keys).reshape(TOKENS, 2).astype(jnp.int32)


def block_levels(key, shape, cuts, low, largest):
    def one(position, parts):
        draws = jax.random.uniform(jax.random.fold_in(jax.random.fold_in(key, 6), position), (parts,), jnp.float32, low / len(cuts), largest / len(cuts))
        return jnp.repeat(jnp.exp(draws), shape[position] // parts).reshape((-1,) + (1,) * (len(shape) - position - 1))

    gain = one(*cuts[0])
    for cut in cuts[1:]:
        gain = gain * one(*cut)
    return gain


def centred(key, extent, scale, most, shards=(), held_as=jnp.bfloat16):
    result = scale * jax.random.normal(key, extent, jnp.float32)
    if shards:
        result = result * block_levels(key, extent, shards, -0.22, 0.18)
    return jnp.clip(result, -most, most).astype(held_as)


def setup_inputs(seed: int = 0) -> dict:
    splits = jax.random.split(jax.random.key(seed), 8)
    return {
        "tokens": centred(splits[0], (TOKENS, D), 1.0, 6.0, ((0, 32), (1, 8))),
        "out_grad": centred(splits[1], (TOKENS, D), 0.5, 3.0, ((0, 32), (1, 8))),
        "expert_ids": draw_expert_ids(jax.random.fold_in(splits[7], 71), 0),
        "gate_probs": jnp.clip(0.25 + 0.75 * jax.random.uniform(splits[3], (TOKENS, 2), jnp.float32) ** block_levels(splits[3], (TOKENS, 2), ((0, 32),), -0.2, 0.2), 0.25, 1.0),
        "w_gate": centred(splits[4], (EXPERTS, D, FF), D ** -0.5, 0.09375, ((0, 32), (1, 8))),
        "w_up": centred(splits[5], (EXPERTS, D, FF), D ** -0.5, 0.09375, ((0, 32), (1, 8))),
        "w_down": centred(splits[6], (EXPERTS, FF, D), FF ** -0.5, 0.1875, ((0, 32), (2, 8))),
    }


def silu_parts(pre_gate):
    sigmoid_gate = jax.nn.sigmoid(pre_gate)
    return pre_gate * sigmoid_gate, sigmoid_gate * (1.0 + pre_gate * (1.0 - sigmoid_gate))


def rounded(values):
    return lax.optimization_barrier(values.astype(jnp.bfloat16)).astype(jnp.float32)


def reference(tokens, out_grad, expert_ids, gate_probs, w_gate, w_up, w_down):
    model_width = tokens.shape[1]
    slab_width = model_width // N_DP
    hidden_width = w_gate.shape[2]
    flat_ids = expert_ids.reshape(-1)
    owner_row = jnp.arange(flat_ids.shape[0], dtype=jnp.int32) // 2
    flat_probs = gate_probs.reshape(-1)
    capacity = N_EXPERT * MOST

    def per_expert(grad_total, expert):
        matches = flat_ids == expert
        chosen = jnp.nonzero(matches, size=capacity, fill_value=0)[0].astype(jnp.int32)
        live_rows = (jnp.arange(capacity, dtype=jnp.int32) < jnp.sum(matches.astype(jnp.int32)))[:, None]
        token_rows = owner_row[chosen]
        gathered = jnp.where(live_rows, tokens[token_rows], jnp.zeros((), tokens.dtype))
        scaled = jnp.where(live_rows, flat_probs[chosen][:, None] * out_grad[token_rows].astype(jnp.float32), 0.0).astype(jnp.bfloat16)
        gate_mat = w_gate[expert]
        up_mat = w_up[expert]
        down_mat = w_down[expert]
        pre_gate = jnp.zeros((capacity, hidden_width), jnp.float32)
        pre_up = jnp.zeros((capacity, hidden_width), jnp.float32)
        grad_act = jnp.zeros((capacity, hidden_width), jnp.float32)
        for block_index in range(N_DP):
            first_col = block_index * slab_width
            last_col = first_col + slab_width
            pre_gate = pre_gate + rounded(jnp.dot(gathered[:, first_col:last_col], gate_mat[first_col:last_col], preferred_element_type=jnp.float32))
            pre_up = pre_up + rounded(jnp.dot(gathered[:, first_col:last_col], up_mat[first_col:last_col], preferred_element_type=jnp.float32))
            grad_act = grad_act + rounded(jnp.dot(scaled[:, first_col:last_col], down_mat[:, first_col:last_col].T, preferred_element_type=jnp.float32))
        active, slope_gate = silu_parts(pre_gate)
        hidden = (active * pre_up).astype(jnp.bfloat16)
        grad_gate = (grad_act * pre_up * slope_gate).astype(jnp.bfloat16)
        grad_up = (grad_act * active).astype(jnp.bfloat16)
        pick_grad = jnp.dot(grad_gate, gate_mat.T, preferred_element_type=jnp.float32) + jnp.dot(grad_up, up_mat.T, preferred_element_type=jnp.float32)
        grad_total = grad_total.at[token_rows].add(jnp.where(live_rows, pick_grad, 0.0))
        gate_grads = jnp.dot(gathered.T, grad_gate, preferred_element_type=jnp.float32)
        up_grads = jnp.dot(gathered.T, grad_up, preferred_element_type=jnp.float32)
        down_grads = jnp.dot(hidden.T, scaled, preferred_element_type=jnp.float32)
        return grad_total, (gate_grads, up_grads, down_grads)

    initial = jnp.zeros(tokens.shape, jnp.float32)
    grad_total, stacked = lax.scan(per_expert, initial, jnp.arange(EXPERTS, dtype=jnp.int32))
    return grad_total.astype(jnp.bfloat16), stacked[0], stacked[1], stacked[2]
```

```python
import jax
import jax.numpy as jnp
from jax import lax
from jax.sharding import PartitionSpec as P

MOST = 32
CHUNKS = 4


contract_rows = (((0,), (0,)), ((), ()))
contract_cols = (((1,), (1,)), ((), ()))


def silu_parts(pre_gate):
    sigmoid_gate = jax.nn.sigmoid(pre_gate)
    return (pre_gate * sigmoid_gate, sigmoid_gate * (1.0 + pre_gate * (1.0 - sigmoid_gate)))


def local_grads(pre_gate, pre_up, grad_act):
    active, slope_gate = silu_parts(pre_gate)
    hidden = (active * pre_up).astype(jnp.bfloat16)
    grad_gate = (grad_act * pre_up * slope_gate).astype(jnp.bfloat16)
    grad_up = (grad_act * active).astype(jnp.bfloat16)
    return (hidden, grad_gate, grad_up)


def shards(tokens, out_grad, expert_ids, gate_probs, w_gate, w_up, w_down):
    tok_rows, slab_width = tokens.shape
    owners = lax.axis_size("expert")
    experts = owners * w_gate.shape[0]
    hidden_width = w_gate.shape[2]
    pick_ids = expert_ids.T.reshape(-1)
    onehot = (pick_ids[:, None] == jnp.arange(experts, dtype=jnp.int32)[None, :]).astype(jnp.int32)
    rank_in = jnp.sum((jnp.cumsum(onehot, axis=0) - 1) * onehot, axis=1)
    slot_of = pick_ids * MOST + rank_in
    placing = (jnp.arange(experts * MOST, dtype=jnp.int32)[:, None] == slot_of[None, :]).astype(
        jnp.bfloat16
    )
    row_pick = jnp.concatenate([tokens, tokens], axis=0)
    grad_pick = jnp.concatenate([out_grad, out_grad], axis=0)
    scaled = (gate_probs.T.reshape(-1)[:, None] * grad_pick.astype(jnp.float32)).astype(
        jnp.bfloat16
    )
    both = jnp.concatenate([row_pick, scaled], axis=1)
    send = (
        jnp.dot(placing, both, preferred_element_type=jnp.float32)
        .astype(jnp.bfloat16)
        .reshape(experts, MOST, 2 * slab_width)
    )
    gate_mat = w_gate[0]
    up_mat = w_up[0]
    down_mat = w_down[0]
    step = MOST // CHUNKS
    gate_grads = jnp.zeros((slab_width, hidden_width), jnp.float32)
    up_grads = jnp.zeros((slab_width, hidden_width), jnp.float32)
    down_grads = jnp.zeros((hidden_width, slab_width), jnp.float32)
    received = []
    partial_list = []
    for c in range(CHUNKS):
        part = send[:, c * step : (c + 1) * step, :]
        arrived = lax.all_to_all(part, "expert", split_axis=0, concat_axis=0, tiled=True)
        flat = arrived.reshape(-1, 2 * slab_width)
        flat_tokens = flat[:, :slab_width]
        flat_grads = flat[:, slab_width:]
        part_gate = jnp.dot(flat_tokens, gate_mat, preferred_element_type=jnp.float32)
        part_up = jnp.dot(flat_tokens, up_mat, preferred_element_type=jnp.float32)
        part_act = lax.dot_general(
            flat_grads, down_mat, contract_cols, preferred_element_type=jnp.float32
        )
        partials = jnp.concatenate([part_gate, part_up, part_act], axis=1).astype(jnp.bfloat16)
        received.append((flat_tokens, flat_grads))
        partial_list.append(partials)
    back = []
    summed = None
    for c in range(CHUNKS):
        flat_tokens, flat_grads = received[c]
        partials = partial_list[c]
        if summed is not None:
            partials, _ = lax.optimization_barrier((partials, summed))
        summed = lax.psum(partials, "dp")
        wide = summed.astype(jnp.float32)
        pre_gate = wide[:, :hidden_width]
        pre_up = wide[:, hidden_width : 2 * hidden_width]
        grad_act = wide[:, 2 * hidden_width :]
        hidden, grad_gate, grad_up = local_grads(pre_gate, pre_up, grad_act)
        slot_grad = lax.dot_general(
            grad_gate, gate_mat, contract_cols, preferred_element_type=jnp.float32
        )
        slot_grad = slot_grad + lax.dot_general(
            grad_up, up_mat, contract_cols, preferred_element_type=jnp.float32
        )
        gate_grads = gate_grads + lax.dot_general(
            flat_tokens, grad_gate, contract_rows, preferred_element_type=jnp.float32
        )
        up_grads = up_grads + lax.dot_general(
            flat_tokens, grad_up, contract_rows, preferred_element_type=jnp.float32
        )
        down_grads = down_grads + lax.dot_general(
            hidden, flat_grads, contract_rows, preferred_element_type=jnp.float32
        )
        returned = lax.all_to_all(
            slot_grad.reshape(experts, step, slab_width).astype(jnp.bfloat16),
            "expert",
            split_axis=0,
            concat_axis=0,
            tiled=True,
        )
        back.append(returned)
    flat_back = jnp.concatenate(back, axis=1).astype(jnp.float32).reshape(experts * MOST, slab_width)
    per_pick = jnp.take(flat_back, slot_of, axis=0)
    token_grad = (per_pick[:tok_rows] + per_pick[tok_rows:]).astype(jnp.bfloat16)
    return (token_grad, gate_grads[None], up_grads[None], down_grads[None])


def solution(mesh):
    in_specs = (
        P("expert", "dp"),
        P("expert", "dp"),
        P("expert", None),
        P("expert", None),
        P("expert", "dp", None),
        P("expert", "dp", None),
        P("expert", None, "dp"),
    )
    out_specs = (
        P("expert", "dp"),
        P("expert", "dp", None),
        P("expert", "dp", None),
        P("expert", None, "dp"),
    )
    return jax.shard_map(shards, mesh=mesh, in_specs=in_specs, out_specs=out_specs, check_vma=False)
```

```python
import jax
import jax.numpy as jnp
from jax import lax
from jax.sharding import PartitionSpec as P

MOST = 32


contract_rows = (((0,), (0,)), ((), ()))
contract_cols = (((1,), (1,)), ((), ()))


def silu_parts(pre_gate):
    sigmoid_gate = jax.nn.sigmoid(pre_gate)
    return (pre_gate * sigmoid_gate, sigmoid_gate * (1.0 + pre_gate * (1.0 - sigmoid_gate)))


def local_grads(pre_gate, pre_up, grad_act):
    active, slope_gate = silu_parts(pre_gate)
    hidden = (active * pre_up).astype(jnp.bfloat16)
    grad_gate = (grad_act * pre_up * slope_gate).astype(jnp.bfloat16)
    grad_up = (grad_act * active).astype(jnp.bfloat16)
    return (hidden, grad_gate, grad_up)


def shards(tokens, out_grad, expert_ids, gate_probs, w_gate, w_up, w_down):
    tok_rows, slab_width = tokens.shape
    owners = lax.axis_size("expert")
    experts = owners * w_gate.shape[0]
    pick_ids = expert_ids.T.reshape(-1)
    onehot = (pick_ids[:, None] == jnp.arange(experts, dtype=jnp.int32)[None, :]).astype(jnp.int32)
    rank_in = jnp.sum((jnp.cumsum(onehot, axis=0) - 1) * onehot, axis=1)
    slot_of = pick_ids * MOST + rank_in
    placing = (jnp.arange(experts * MOST, dtype=jnp.int32)[:, None] == slot_of[None, :]).astype(
        jnp.bfloat16
    )
    row_pick = jnp.concatenate([tokens, tokens], axis=0)
    grad_pick = jnp.concatenate([out_grad, out_grad], axis=0)
    scaled = (gate_probs.T.reshape(-1)[:, None] * grad_pick.astype(jnp.float32)).astype(
        jnp.bfloat16
    )
    hidden_width = w_gate.shape[2]
    gate_mat = w_gate[0]
    up_mat = w_up[0]
    down_mat = w_down[0]
    send_tokens = (
        jnp.dot(placing, row_pick, preferred_element_type=jnp.float32)
        .astype(jnp.bfloat16)
        .reshape(experts, MOST, slab_width)
    )
    arrived_tokens = lax.all_to_all(send_tokens, "expert", split_axis=0, concat_axis=0, tiled=True)
    flat_tokens = arrived_tokens.reshape(-1, slab_width)
    part_gate = jnp.dot(flat_tokens, gate_mat, preferred_element_type=jnp.float32)
    part_up = jnp.dot(flat_tokens, up_mat, preferred_element_type=jnp.float32)
    gate_up = jnp.concatenate([part_gate, part_up], axis=1).astype(jnp.bfloat16)
    summed = lax.psum(gate_up, "dp").astype(jnp.float32)
    pre_gate = summed[:, :hidden_width]
    pre_up = summed[:, hidden_width:]
    send_grads = (
        jnp.dot(placing, scaled, preferred_element_type=jnp.float32)
        .astype(jnp.bfloat16)
        .reshape(experts, MOST, slab_width)
    )
    arrived_grads = lax.all_to_all(send_grads, "expert", split_axis=0, concat_axis=0, tiled=True)
    flat_grads = arrived_grads.reshape(-1, slab_width)
    part_act = lax.dot_general(
        flat_grads, down_mat, contract_cols, preferred_element_type=jnp.float32
    ).astype(jnp.bfloat16)
    n_dp = lax.axis_size("dp")
    rows = part_act.shape[0]
    pieces = part_act.reshape(rows, n_dp, hidden_width // n_dp).transpose(1, 0, 2)
    got = lax.all_to_all(pieces, "dp", split_axis=0, concat_axis=0, tiled=True)
    mine = jnp.sum(got.astype(jnp.float32), axis=0).astype(jnp.bfloat16)
    spread = jnp.broadcast_to(mine[None], (n_dp,) + mine.shape)
    gathered = lax.all_to_all(spread, "dp", split_axis=0, concat_axis=0, tiled=True)
    grad_act = gathered.transpose(1, 0, 2).reshape(rows, hidden_width).astype(jnp.float32)
    hidden, grad_gate, grad_up = local_grads(pre_gate, pre_up, grad_act)
    slot_grad = lax.dot_general(
        grad_gate, gate_mat, contract_cols, preferred_element_type=jnp.float32
    )
    slot_grad = slot_grad + lax.dot_general(
        grad_up, up_mat, contract_cols, preferred_element_type=jnp.float32
    )
    gate_grads = lax.dot_general(
        flat_tokens, grad_gate, contract_rows, preferred_element_type=jnp.float32
    )[None]
    up_grads = lax.dot_general(
        flat_tokens, grad_up, contract_rows, preferred_element_type=jnp.float32
    )[None]
    down_grads = lax.dot_general(
        hidden, flat_grads, contract_rows, preferred_element_type=jnp.float32
    )[None]
    returned = lax.all_to_all(
        slot_grad.reshape(experts, MOST, slab_width).astype(jnp.bfloat16),
        "expert",
        split_axis=0,
        concat_axis=0,
        tiled=True,
    ).astype(jnp.float32)
    flat_back = returned.reshape(experts * MOST, slab_width)
    per_pick = jnp.take(flat_back, slot_of, axis=0)
    token_grad = (per_pick[:tok_rows] + per_pick[tok_rows:]).astype(jnp.bfloat16)
    return (token_grad, gate_grads, up_grads, down_grads)


def solution(mesh):
    in_specs = (
        P("expert", "dp"),
        P("expert", "dp"),
        P("expert", None),
        P("expert", None),
        P("expert", "dp", None),
        P("expert", "dp", None),
        P("expert", None, "dp"),
    )
    out_specs = (
        P("expert", "dp"),
        P("expert", "dp", None),
        P("expert", "dp", None),
        P("expert", None, "dp"),
    )
    return jax.shard_map(shards, mesh=mesh, in_specs=in_specs, out_specs=out_specs, check_vma=False)
```

```python
import jax
import jax.numpy as jnp
from jax import lax
from jax.sharding import PartitionSpec as P

MOST = 32


contract_rows = (((0,), (0,)), ((), ()))
contract_cols = (((1,), (1,)), ((), ()))


def silu_parts(pre_gate):
    sigmoid_gate = jax.nn.sigmoid(pre_gate)
    return (pre_gate * sigmoid_gate, sigmoid_gate * (1.0 + pre_gate * (1.0 - sigmoid_gate)))


def local_grads(pre_gate, pre_up, grad_act):
    active, slope_gate = silu_parts(pre_gate)
    hidden = (active * pre_up).astype(jnp.bfloat16)
    grad_gate = (grad_act * pre_up * slope_gate).astype(jnp.bfloat16)
    grad_up = (grad_act * active).astype(jnp.bfloat16)
    return (hidden, grad_gate, grad_up)


def shards(tokens, out_grad, expert_ids, gate_probs, w_gate, w_up, w_down):
    tok_rows, slab_width = tokens.shape
    owners = lax.axis_size("expert")
    experts = owners * w_gate.shape[0]
    pick_ids = expert_ids.T.reshape(-1)
    onehot = (pick_ids[:, None] == jnp.arange(experts, dtype=jnp.int32)[None, :]).astype(jnp.int32)
    rank_in = jnp.sum((jnp.cumsum(onehot, axis=0) - 1) * onehot, axis=1)
    slot_of = pick_ids * MOST + rank_in
    placing = (jnp.arange(experts * MOST, dtype=jnp.int32)[:, None] == slot_of[None, :]).astype(
        jnp.bfloat16
    )
    row_pick = jnp.concatenate([tokens, tokens], axis=0)
    grad_pick = jnp.concatenate([out_grad, out_grad], axis=0)
    scaled = (gate_probs.T.reshape(-1)[:, None] * grad_pick.astype(jnp.float32)).astype(
        jnp.bfloat16
    )
    hidden_width = w_gate.shape[2]
    gate_mat = w_gate[0]
    up_mat = w_up[0]
    down_mat = w_down[0]
    send_tokens = (
        jnp.dot(placing, row_pick, preferred_element_type=jnp.float32)
        .astype(jnp.bfloat16)
        .reshape(experts, MOST, slab_width)
    )
    arrived_tokens = lax.all_to_all(send_tokens, "expert", split_axis=0, concat_axis=0, tiled=True)
    flat_tokens = arrived_tokens.reshape(-1, slab_width)
    part_gate = jnp.dot(flat_tokens, gate_mat, preferred_element_type=jnp.float32)
    part_up = jnp.dot(flat_tokens, up_mat, preferred_element_type=jnp.float32)
    gate_up = jnp.concatenate([part_gate, part_up], axis=1).astype(jnp.bfloat16)
    summed = lax.psum(gate_up, "dp").astype(jnp.float32)
    pre_gate = summed[:, :hidden_width]
    pre_up = summed[:, hidden_width:]
    send_grads = (
        jnp.dot(placing, scaled, preferred_element_type=jnp.float32)
        .astype(jnp.bfloat16)
        .reshape(experts, MOST, slab_width)
    )
    arrived_grads = lax.all_to_all(send_grads, "expert", split_axis=0, concat_axis=0, tiled=True)
    flat_grads = arrived_grads.reshape(-1, slab_width)
    part_act = lax.dot_general(
        flat_grads, down_mat, contract_cols, preferred_element_type=jnp.float32
    ).astype(jnp.bfloat16)
    n_dp = lax.axis_size("dp")
    rows = part_act.shape[0]
    pieces = part_act.reshape(rows, n_dp, hidden_width // n_dp).transpose(1, 0, 2)
    got = lax.all_to_all(pieces, "dp", split_axis=0, concat_axis=0, tiled=True)
    mine = jnp.sum(got.astype(jnp.float32), axis=0).astype(jnp.bfloat16)
    spread = jnp.broadcast_to(mine[None], (n_dp,) + mine.shape)
    gathered = lax.all_to_all(spread, "dp", split_axis=0, concat_axis=0, tiled=True)
    grad_act = gathered.transpose(1, 0, 2).reshape(rows, hidden_width).astype(jnp.float32)
    hidden, grad_gate, grad_up = lax.optimization_barrier(local_grads(pre_gate, pre_up, grad_act))
    slot_grad = lax.dot_general(
        grad_gate, gate_mat, contract_cols, preferred_element_type=jnp.float32
    )
    slot_grad = slot_grad + lax.dot_general(
        grad_up, up_mat, contract_cols, preferred_element_type=jnp.float32
    )
    gate_grads = lax.dot_general(
        flat_tokens, grad_gate, contract_rows, preferred_element_type=jnp.float32
    )[None]
    up_grads = lax.dot_general(
        flat_tokens, grad_up, contract_rows, preferred_element_type=jnp.float32
    )[None]
    down_grads = lax.dot_general(
        hidden, flat_grads, contract_rows, preferred_element_type=jnp.float32
    )[None]
    returned = lax.all_to_all(
        slot_grad.reshape(experts, MOST, slab_width).astype(jnp.bfloat16),
        "expert",
        split_axis=0,
        concat_axis=0,
        tiled=True,
    )
    flat_back = returned.reshape(experts * MOST, slab_width)
    per_pick = lax.dot_general(placing, flat_back, contract_rows, preferred_element_type=jnp.float32)
    token_grad = (per_pick[:tok_rows] + per_pick[tok_rows:]).astype(jnp.bfloat16)
    return (token_grad, gate_grads, up_grads, down_grads)


def solution(mesh):
    in_specs = (
        P("expert", "dp"),
        P("expert", "dp"),
        P("expert", None),
        P("expert", None),
        P("expert", "dp", None),
        P("expert", "dp", None),
        P("expert", None, "dp"),
    )
    out_specs = (
        P("expert", "dp"),
        P("expert", "dp", None),
        P("expert", "dp", None),
        P("expert", None, "dp"),
    )
    return jax.shard_map(shards, mesh=mesh, in_specs=in_specs, out_specs=out_specs, check_vma=False)
```

```python
import jax
import jax.numpy as jnp
from jax import lax
from jax.sharding import PartitionSpec as P

MOST = 32


contract_rows = (((0,), (0,)), ((), ()))
contract_cols = (((1,), (1,)), ((), ()))


def silu_parts(pre_gate):
    sigmoid_gate = jax.nn.sigmoid(pre_gate)
    return (pre_gate * sigmoid_gate, sigmoid_gate * (1.0 + pre_gate * (1.0 - sigmoid_gate)))


def local_grads(pre_gate, pre_up, grad_act):
    active, slope_gate = silu_parts(pre_gate)
    hidden = (active * pre_up).astype(jnp.bfloat16)
    grad_gate = (grad_act * pre_up * slope_gate).astype(jnp.bfloat16)
    grad_up = (grad_act * active).astype(jnp.bfloat16)
    return (hidden, grad_gate, grad_up)


def shards(tokens, out_grad, expert_ids, gate_probs, w_gate, w_up, w_down):
    tok_rows, slab_width = tokens.shape
    owners = lax.axis_size("expert")
    experts = owners * w_gate.shape[0]
    pick_ids = expert_ids.T.reshape(-1)
    onehot = (pick_ids[:, None] == jnp.arange(experts, dtype=jnp.int32)[None, :]).astype(jnp.int32)
    rank_in = jnp.sum((jnp.cumsum(onehot, axis=0) - 1) * onehot, axis=1)
    slot_of = pick_ids * MOST + rank_in
    placing = (jnp.arange(experts * MOST, dtype=jnp.int32)[:, None] == slot_of[None, :]).astype(
        jnp.bfloat16
    )
    row_pick = jnp.concatenate([tokens, tokens], axis=0)
    grad_pick = jnp.concatenate([out_grad, out_grad], axis=0)
    scaled = (gate_probs.T.reshape(-1)[:, None] * grad_pick.astype(jnp.float32)).astype(
        jnp.bfloat16
    )
    both = jnp.concatenate([row_pick, scaled], axis=1)
    send = (
        jnp.dot(placing, both, preferred_element_type=jnp.float32)
        .astype(jnp.bfloat16)
        .reshape(experts, MOST, 2 * slab_width)
    )
    arrived = lax.all_to_all(send, "expert", split_axis=0, concat_axis=0, tiled=True)
    arrived_tokens = arrived[:, :, :slab_width]
    arrived_grads = arrived[:, :, slab_width:]
    flat_tokens = arrived_tokens.reshape(-1, slab_width)
    flat_grads = arrived_grads.reshape(-1, slab_width)
    gate_mat = w_gate[0]
    up_mat = w_up[0]
    down_mat = w_down[0]
    part_gate = jnp.dot(flat_tokens, gate_mat, preferred_element_type=jnp.float32)
    part_up = jnp.dot(flat_tokens, up_mat, preferred_element_type=jnp.float32)
    part_act = lax.dot_general(
        flat_grads, down_mat, contract_cols, preferred_element_type=jnp.float32
    )
    pre_gate, pre_up, grad_act = (
        lax.psum(part_gate.astype(jnp.bfloat16), "dp").astype(jnp.float32),
        lax.psum(part_up.astype(jnp.bfloat16), "dp").astype(jnp.float32),
        lax.psum(part_act.astype(jnp.bfloat16), "dp").astype(jnp.float32),
    )
    hidden, grad_gate, grad_up = lax.optimization_barrier(local_grads(pre_gate, pre_up, grad_act))
    slot_grad = lax.dot_general(
        grad_gate, gate_mat, contract_cols, preferred_element_type=jnp.float32
    )
    slot_grad = slot_grad + lax.dot_general(
        grad_up, up_mat, contract_cols, preferred_element_type=jnp.float32
    )
    gate_grads = lax.dot_general(
        flat_tokens, grad_gate, contract_rows, preferred_element_type=jnp.float32
    )[None]
    up_grads = lax.dot_general(
        flat_tokens, grad_up, contract_rows, preferred_element_type=jnp.float32
    )[None]
    down_grads = lax.dot_general(
        hidden, flat_grads, contract_rows, preferred_element_type=jnp.float32
    )[None]
    returned = lax.all_to_all(
        slot_grad.reshape(experts, MOST, slab_width).astype(jnp.bfloat16),
        "expert",
        split_axis=0,
        concat_axis=0,
        tiled=True,
    )
    flat_back = returned.reshape(experts * MOST, slab_width)
    per_pick = lax.dot_general(placing, flat_back, contract_rows, preferred_element_type=jnp.float32)
    token_grad = (per_pick[:tok_rows] + per_pick[tok_rows:]).astype(jnp.bfloat16)
    return (token_grad, gate_grads, up_grads, down_grads)


def solution(mesh):
    in_specs = (
        P("expert", "dp"),
        P("expert", "dp"),
        P("expert", None),
        P("expert", None),
        P("expert", "dp", None),
        P("expert", "dp", None),
        P("expert", None, "dp"),
    )
    out_specs = (
        P("expert", "dp"),
        P("expert", "dp", None),
        P("expert", "dp", None),
        P("expert", None, "dp"),
    )
    return jax.shard_map(shards, mesh=mesh, in_specs=in_specs, out_specs=out_specs, check_vma=False)
```

```python
import jax
import jax.numpy as jnp
from jax import lax
from jax.sharding import PartitionSpec as P

MOST = 32


contract_rows = (((0,), (0,)), ((), ()))
contract_cols = (((1,), (1,)), ((), ()))


def silu_parts(pre_gate):
    sigmoid_gate = jax.nn.sigmoid(pre_gate)
    return (pre_gate * sigmoid_gate, sigmoid_gate * (1.0 + pre_gate * (1.0 - sigmoid_gate)))


def local_grads(pre_gate, pre_up, grad_act):
    active, slope_gate = silu_parts(pre_gate)
    hidden = (active * pre_up).astype(jnp.bfloat16)
    grad_gate = (grad_act * pre_up * slope_gate).astype(jnp.bfloat16)
    grad_up = (grad_act * active).astype(jnp.bfloat16)
    return (hidden, grad_gate, grad_up)


def shards(tokens, out_grad, expert_ids, gate_probs, w_gate, w_up, w_down):
    tok_rows, slab_width = tokens.shape
    owners = lax.axis_size("expert")
    experts = owners * w_gate.shape[0]
    pick_ids = expert_ids.T.reshape(-1)
    onehot = (pick_ids[:, None] == jnp.arange(experts, dtype=jnp.int32)[None, :]).astype(jnp.int32)
    rank_in = jnp.sum((jnp.cumsum(onehot, axis=0) - 1) * onehot, axis=1)
    slot_of = pick_ids * MOST + rank_in
    placing = (jnp.arange(experts * MOST, dtype=jnp.int32)[:, None] == slot_of[None, :]).astype(
        jnp.bfloat16
    )
    row_pick = jnp.concatenate([tokens, tokens], axis=0)
    grad_pick = jnp.concatenate([out_grad, out_grad], axis=0)
    scaled = (gate_probs.T.reshape(-1)[:, None] * grad_pick.astype(jnp.float32)).astype(
        jnp.bfloat16
    )
    both = jnp.concatenate([row_pick, scaled], axis=1)
    send = (
        jnp.dot(placing, both, preferred_element_type=jnp.float32)
        .astype(jnp.bfloat16)
        .reshape(experts, MOST, 2 * slab_width)
    )
    arrived = lax.all_to_all(send, "expert", split_axis=0, concat_axis=0, tiled=True)
    arrived_tokens = arrived[:, :, :slab_width]
    arrived_grads = arrived[:, :, slab_width:]
    flat_tokens = arrived_tokens.reshape(-1, slab_width)
    flat_grads = arrived_grads.reshape(-1, slab_width)
    gate_mat = w_gate[0]
    up_mat = w_up[0]
    down_mat = w_down[0]
    part_gate = jnp.dot(flat_tokens, gate_mat, preferred_element_type=jnp.float32)
    part_up = jnp.dot(flat_tokens, up_mat, preferred_element_type=jnp.float32)
    part_act = lax.dot_general(
        flat_grads, down_mat, contract_cols, preferred_element_type=jnp.float32
    )
    pre_gate, pre_up, grad_act = (
        lax.psum(part_gate.astype(jnp.bfloat16), "dp").astype(jnp.float32),
        lax.psum(part_up.astype(jnp.bfloat16), "dp").astype(jnp.float32),
        lax.psum(part_act.astype(jnp.bfloat16), "dp").astype(jnp.float32),
    )
    hidden, grad_gate, grad_up = local_grads(pre_gate, pre_up, grad_act)
    grad_gate, grad_up = lax.optimization_barrier((grad_gate, grad_up))
    slot_grad = lax.dot_general(
        grad_gate, gate_mat, contract_cols, preferred_element_type=jnp.float32
    )
    slot_grad = slot_grad + lax.dot_general(
        grad_up, up_mat, contract_cols, preferred_element_type=jnp.float32
    )
    gate_grads = lax.dot_general(
        flat_tokens, grad_gate, contract_rows, preferred_element_type=jnp.float32
    )[None]
    up_grads = lax.dot_general(
        flat_tokens, grad_up, contract_rows, preferred_element_type=jnp.float32
    )[None]
    down_grads = lax.dot_general(
        hidden, flat_grads, contract_rows, preferred_element_type=jnp.float32
    )[None]
    returned = lax.all_to_all(
        slot_grad.reshape(experts, MOST, slab_width).astype(jnp.bfloat16),
        "expert",
        split_axis=0,
        concat_axis=0,
        tiled=True,
    )
    flat_back = returned.reshape(experts * MOST, slab_width)
    per_pick = lax.dot_general(placing, flat_back, contract_rows, preferred_element_type=jnp.float32)
    token_grad = (per_pick[:tok_rows] + per_pick[tok_rows:]).astype(jnp.bfloat16)
    return (token_grad, gate_grads, up_grads, down_grads)


def solution(mesh):
    in_specs = (
        P("expert", "dp"),
        P("expert", "dp"),
        P("expert", None),
        P("expert", None),
        P("expert", "dp", None),
        P("expert", "dp", None),
        P("expert", None, "dp"),
    )
    out_specs = (
        P("expert", "dp"),
        P("expert", "dp", None),
        P("expert", "dp", None),
        P("expert", None, "dp"),
    )
    return jax.shard_map(shards, mesh=mesh, in_specs=in_specs, out_specs=out_specs, check_vma=False)
```

```python
import jax
import jax.numpy as jnp
from jax import lax
from jax.sharding import PartitionSpec as P

MOST = 32


contract_rows = (((0,), (0,)), ((), ()))
contract_cols = (((1,), (1,)), ((), ()))


def silu_parts(pre_gate):
    sigmoid_gate = jax.nn.sigmoid(pre_gate)
    return (pre_gate * sigmoid_gate, sigmoid_gate * (1.0 + pre_gate * (1.0 - sigmoid_gate)))


def local_grads(pre_gate, pre_up, grad_act):
    active, slope_gate = silu_parts(pre_gate)
    hidden = (active * pre_up).astype(jnp.bfloat16)
    grad_gate = (grad_act * pre_up * slope_gate).astype(jnp.bfloat16)
    grad_up = (grad_act * active).astype(jnp.bfloat16)
    return (hidden, grad_gate, grad_up)


def shards(tokens, out_grad, expert_ids, gate_probs, w_gate, w_up, w_down):
    tok_rows, slab_width = tokens.shape
    owners = lax.axis_size("expert")
    experts = owners * w_gate.shape[0]
    pick_ids = expert_ids.T.reshape(-1)
    onehot = (pick_ids[:, None] == jnp.arange(experts, dtype=jnp.int32)[None, :]).astype(jnp.int32)
    rank_in = jnp.sum((jnp.cumsum(onehot, axis=0) - 1) * onehot, axis=1)
    slot_of = pick_ids * MOST + rank_in
    placing = (jnp.arange(experts * MOST, dtype=jnp.int32)[:, None] == slot_of[None, :]).astype(
        jnp.bfloat16
    )
    row_pick = jnp.concatenate([tokens, tokens], axis=0)
    grad_pick = jnp.concatenate([out_grad, out_grad], axis=0)
    scaled = (gate_probs.T.reshape(-1)[:, None] * grad_pick.astype(jnp.float32)).astype(
        jnp.bfloat16
    )
    both = jnp.concatenate([row_pick, scaled], axis=1)
    send = (
        jnp.dot(placing, both, preferred_element_type=jnp.float32)
        .astype(jnp.bfloat16)
        .reshape(experts, MOST, 2 * slab_width)
    )
    hidden_width = w_gate.shape[2]
    n_dp = lax.axis_size("dp")
    gate_mat = w_gate[0]
    up_mat = w_up[0]
    down_mat = w_down[0]
    split = MOST - MOST // 4

    def partials_of(chunk):
        arrived = lax.all_to_all(chunk, "expert", split_axis=0, concat_axis=0, tiled=True)
        flat = arrived.reshape(-1, 2 * slab_width)
        flat_tokens = flat[:, :slab_width]
        flat_grads = flat[:, slab_width:]
        part_gate = jnp.dot(flat_tokens, gate_mat, preferred_element_type=jnp.float32)
        part_up = jnp.dot(flat_tokens, up_mat, preferred_element_type=jnp.float32)
        part_act = lax.dot_general(
            flat_grads, down_mat, contract_cols, preferred_element_type=jnp.float32
        )
        partials = jnp.concatenate([part_gate, part_up, part_act], axis=1).astype(jnp.bfloat16)
        return flat_tokens, flat_grads, partials

    tokens_a, grads_a, partials_a = partials_of(send[:, :split])
    summed_a = lax.psum(partials_a, "dp")
    tokens_b, grads_b, partials_b = partials_of(send[:, split:])
    rows_b, width = partials_b.shape
    pieces = partials_b.reshape(rows_b, n_dp, width // n_dp).transpose(1, 0, 2)
    got = lax.all_to_all(pieces, "dp", split_axis=0, concat_axis=0, tiled=True)
    mine = jnp.sum(got.astype(jnp.float32), axis=0).astype(jnp.bfloat16)
    spread = jnp.broadcast_to(mine[None], (n_dp,) + mine.shape)
    gathered = lax.all_to_all(spread, "dp", split_axis=0, concat_axis=0, tiled=True)
    summed_b = gathered.transpose(1, 0, 2).reshape(rows_b, width)

    gate_grads = jnp.zeros((slab_width, hidden_width), jnp.float32)
    up_grads = jnp.zeros((slab_width, hidden_width), jnp.float32)
    down_grads = jnp.zeros((hidden_width, slab_width), jnp.float32)
    back = []
    for flat_tokens, flat_grads, summed in ((tokens_a, grads_a, summed_a), (tokens_b, grads_b, summed_b)):
        wide = summed.astype(jnp.float32)
        pre_gate = wide[:, :hidden_width]
        pre_up = wide[:, hidden_width : 2 * hidden_width]
        grad_act = wide[:, 2 * hidden_width :]
        hidden, grad_gate, grad_up = local_grads(pre_gate, pre_up, grad_act)
        grad_gate, grad_up = lax.optimization_barrier((grad_gate, grad_up))
        slot_grad = lax.dot_general(
            grad_gate, gate_mat, contract_cols, preferred_element_type=jnp.float32
        )
        slot_grad = slot_grad + lax.dot_general(
            grad_up, up_mat, contract_cols, preferred_element_type=jnp.float32
        )
        back.append(
            lax.all_to_all(
                slot_grad.reshape(experts, -1, slab_width).astype(jnp.bfloat16),
                "expert",
                split_axis=0,
                concat_axis=0,
                tiled=True,
            )
        )
        gate_grads = gate_grads + lax.dot_general(
            flat_tokens, grad_gate, contract_rows, preferred_element_type=jnp.float32
        )
        up_grads = up_grads + lax.dot_general(
            flat_tokens, grad_up, contract_rows, preferred_element_type=jnp.float32
        )
        down_grads = down_grads + lax.dot_general(
            hidden, flat_grads, contract_rows, preferred_element_type=jnp.float32
        )
    flat_back = jnp.concatenate(back, axis=1).reshape(experts * MOST, slab_width)
    per_pick = lax.dot_general(placing, flat_back, contract_rows, preferred_element_type=jnp.float32)
    token_grad = (per_pick[:tok_rows] + per_pick[tok_rows:]).astype(jnp.bfloat16)
    gate_grads = gate_grads[None]
    up_grads = up_grads[None]
    down_grads = down_grads[None]
    return (token_grad, gate_grads, up_grads, down_grads)


def solution(mesh):
    in_specs = (
        P("expert", "dp"),
        P("expert", "dp"),
        P("expert", None),
        P("expert", None),
        P("expert", "dp", None),
        P("expert", "dp", None),
        P("expert", None, "dp"),
    )
    out_specs = (
        P("expert", "dp"),
        P("expert", "dp", None),
        P("expert", "dp", None),
        P("expert", None, "dp"),
    )
    return jax.shard_map(shards, mesh=mesh, in_specs=in_specs, out_specs=out_specs, check_vma=False)
```

```python
import jax
import jax.numpy as jnp
from jax import lax
from jax.sharding import PartitionSpec as P

MOST = 32


contract_rows = (((0,), (0,)), ((), ()))
contract_cols = (((1,), (1,)), ((), ()))


def silu_parts(pre_gate):
    sigmoid_gate = jax.nn.sigmoid(pre_gate)
    return (pre_gate * sigmoid_gate, sigmoid_gate * (1.0 + pre_gate * (1.0 - sigmoid_gate)))


def local_grads(pre_gate, pre_up, grad_act):
    active, slope_gate = silu_parts(pre_gate)
    hidden = (active * pre_up).astype(jnp.bfloat16)
    grad_gate = (grad_act * pre_up * slope_gate).astype(jnp.bfloat16)
    grad_up = (grad_act * active).astype(jnp.bfloat16)
    return (hidden, grad_gate, grad_up)


def shards(tokens, out_grad, expert_ids, gate_probs, w_gate, w_up, w_down):
    tok_rows, slab_width = tokens.shape
    owners = lax.axis_size("expert")
    experts = owners * w_gate.shape[0]
    pick_ids = expert_ids.T.reshape(-1)
    onehot = (pick_ids[:, None] == jnp.arange(experts, dtype=jnp.int32)[None, :]).astype(jnp.int32)
    rank_in = jnp.sum((jnp.cumsum(onehot, axis=0) - 1) * onehot, axis=1)
    slot_of = pick_ids * MOST + rank_in
    placing = (jnp.arange(experts * MOST, dtype=jnp.int32)[:, None] == slot_of[None, :]).astype(
        jnp.bfloat16
    )
    row_pick = jnp.concatenate([tokens, tokens], axis=0)
    grad_pick = jnp.concatenate([out_grad, out_grad], axis=0)
    scaled = (gate_probs.T.reshape(-1)[:, None] * grad_pick.astype(jnp.float32)).astype(
        jnp.bfloat16
    )
    both = jnp.concatenate([row_pick, scaled], axis=1)
    send = (
        jnp.dot(placing, both, preferred_element_type=jnp.float32)
        .astype(jnp.bfloat16)
        .reshape(experts, MOST, 2 * slab_width)
    )
    arrived = lax.all_to_all(send, "expert", split_axis=0, concat_axis=0, tiled=True)
    arrived_tokens = arrived[:, :, :slab_width]
    arrived_grads = arrived[:, :, slab_width:]
    flat_tokens = arrived_tokens.reshape(-1, slab_width)
    flat_grads = arrived_grads.reshape(-1, slab_width)
    gate_mat = w_gate[0]
    up_mat = w_up[0]
    down_mat = w_down[0]
    part_gate = jnp.dot(flat_tokens, gate_mat, preferred_element_type=jnp.float32)
    part_up = jnp.dot(flat_tokens, up_mat, preferred_element_type=jnp.float32)
    part_act = lax.dot_general(
        flat_grads, down_mat, contract_cols, preferred_element_type=jnp.float32
    )
    pre_gate, pre_up, grad_act = (
        lax.psum(part_gate, "dp"),
        lax.psum(part_up, "dp"),
        lax.psum(part_act, "dp"),
    )
    hidden, grad_gate, grad_up = local_grads(pre_gate, pre_up, grad_act)
    grad_gate, grad_up = lax.optimization_barrier((grad_gate, grad_up))
    slot_grad = lax.dot_general(
        grad_gate, gate_mat, contract_cols, preferred_element_type=jnp.float32
    )
    slot_grad = slot_grad + lax.dot_general(
        grad_up, up_mat, contract_cols, preferred_element_type=jnp.float32
    )
    gate_grads = lax.dot_general(
        flat_tokens, grad_gate, contract_rows, preferred_element_type=jnp.float32
    )[None]
    up_grads = lax.dot_general(
        flat_tokens, grad_up, contract_rows, preferred_element_type=jnp.float32
    )[None]
    down_grads = lax.dot_general(
        hidden, flat_grads, contract_rows, preferred_element_type=jnp.float32
    )[None]
    returned = lax.all_to_all(
        slot_grad.reshape(experts, MOST, slab_width).astype(jnp.bfloat16),
        "expert",
        split_axis=0,
        concat_axis=0,
        tiled=True,
    )
    flat_back = returned.reshape(experts * MOST, slab_width)
    per_pick = lax.dot_general(placing, flat_back, contract_rows, preferred_element_type=jnp.float32)
    token_grad = (per_pick[:tok_rows] + per_pick[tok_rows:]).astype(jnp.bfloat16)
    return (token_grad, gate_grads, up_grads, down_grads)


def solution(mesh):
    in_specs = (
        P("expert", "dp"),
        P("expert", "dp"),
        P("expert", None),
        P("expert", None),
        P("expert", "dp", None),
        P("expert", "dp", None),
        P("expert", None, "dp"),
    )
    out_specs = (
        P("expert", "dp"),
        P("expert", "dp", None),
        P("expert", "dp", None),
        P("expert", None, "dp"),
    )
    return jax.shard_map(shards, mesh=mesh, in_specs=in_specs, out_specs=out_specs, check_vma=False)
```

```python
import jax
import jax.numpy as jnp
from jax import lax
from jax.sharding import PartitionSpec as P

MOST = 32


contract_rows = (((0,), (0,)), ((), ()))
contract_cols = (((1,), (1,)), ((), ()))


def silu_parts(pre_gate):
    sigmoid_gate = jax.nn.sigmoid(pre_gate)
    return (pre_gate * sigmoid_gate, sigmoid_gate * (1.0 + pre_gate * (1.0 - sigmoid_gate)))


def local_grads(pre_gate, pre_up, grad_act):
    active, slope_gate = silu_parts(pre_gate)
    hidden = (active * pre_up).astype(jnp.bfloat16)
    grad_gate = (grad_act * pre_up * slope_gate).astype(jnp.bfloat16)
    grad_up = (grad_act * active).astype(jnp.bfloat16)
    return (hidden, grad_gate, grad_up)


def shards(tokens, out_grad, expert_ids, gate_probs, w_gate, w_up, w_down):
    tok_rows, slab_width = tokens.shape
    owners = lax.axis_size("expert")
    experts = owners * w_gate.shape[0]
    pick_ids = expert_ids.T.reshape(-1)
    onehot = (pick_ids[:, None] == jnp.arange(experts, dtype=jnp.int32)[None, :]).astype(jnp.int32)
    rank_in = jnp.sum((jnp.cumsum(onehot, axis=0) - 1) * onehot, axis=1)
    slot_of = pick_ids * MOST + rank_in
    placing = (jnp.arange(experts * MOST, dtype=jnp.int32)[:, None] == slot_of[None, :]).astype(
        jnp.bfloat16
    )
    row_pick = jnp.concatenate([tokens, tokens], axis=0)
    grad_pick = jnp.concatenate([out_grad, out_grad], axis=0)
    scaled = (gate_probs.T.reshape(-1)[:, None] * grad_pick.astype(jnp.float32)).astype(
        jnp.bfloat16
    )
    both = jnp.concatenate([row_pick, scaled], axis=1)
    send = (
        jnp.dot(placing, both, preferred_element_type=jnp.float32)
        .astype(jnp.bfloat16)
        .reshape(experts, MOST, 2 * slab_width)
    )
    arrived = lax.all_to_all(send, "expert", split_axis=0, concat_axis=0, tiled=True)
    arrived_tokens = arrived[:, :, :slab_width]
    arrived_grads = arrived[:, :, slab_width:]
    flat_tokens = arrived_tokens.reshape(-1, slab_width)
    flat_grads = arrived_grads.reshape(-1, slab_width)
    gate_mat = w_gate[0]
    up_mat = w_up[0]
    down_mat = w_down[0]
    hidden_width = gate_mat.shape[1]
    gate_up_mat = jnp.concatenate([gate_mat, up_mat], axis=1)
    part_gate_up = jnp.dot(flat_tokens, gate_up_mat, preferred_element_type=jnp.float32)
    part_gate = part_gate_up[:, :hidden_width]
    part_up = part_gate_up[:, hidden_width:]
    part_act = lax.dot_general(
        flat_grads, down_mat, contract_cols, preferred_element_type=jnp.float32
    )
    pre_gate, pre_up, grad_act = (
        lax.psum(part_gate.astype(jnp.bfloat16), "dp").astype(jnp.float32),
        lax.psum(part_up.astype(jnp.bfloat16), "dp").astype(jnp.float32),
        lax.psum(part_act.astype(jnp.bfloat16), "dp").astype(jnp.float32),
    )
    hidden, grad_gate, grad_up = local_grads(pre_gate, pre_up, grad_act)
    grad_gate, grad_up = lax.optimization_barrier((grad_gate, grad_up))
    slot_grad = lax.dot_general(
        jnp.concatenate([grad_gate, grad_up], axis=1),
        gate_up_mat,
        contract_cols,
        preferred_element_type=jnp.float32,
    )
    gate_grads = lax.dot_general(
        flat_tokens, grad_gate, contract_rows, preferred_element_type=jnp.float32
    )[None]
    up_grads = lax.dot_general(
        flat_tokens, grad_up, contract_rows, preferred_element_type=jnp.float32
    )[None]
    down_grads = lax.dot_general(
        hidden, flat_grads, contract_rows, preferred_element_type=jnp.float32
    )[None]
    returned = lax.all_to_all(
        slot_grad.reshape(experts, MOST, slab_width).astype(jnp.bfloat16),
        "expert",
        split_axis=0,
        concat_axis=0,
        tiled=True,
    )
    flat_back = returned.reshape(experts * MOST, slab_width)
    per_pick = lax.dot_general(placing, flat_back, contract_rows, preferred_element_type=jnp.float32)
    token_grad = (per_pick[:tok_rows] + per_pick[tok_rows:]).astype(jnp.bfloat16)
    return (token_grad, gate_grads, up_grads, down_grads)


def solution(mesh):
    in_specs = (
        P("expert", "dp"),
        P("expert", "dp"),
        P("expert", None),
        P("expert", None),
        P("expert", "dp", None),
        P("expert", "dp", None),
        P("expert", None, "dp"),
    )
    out_specs = (
        P("expert", "dp"),
        P("expert", "dp", None),
        P("expert", "dp", None),
        P("expert", None, "dp"),
    )
    return jax.shard_map(shards, mesh=mesh, in_specs=in_specs, out_specs=out_specs, check_vma=False)
```

```python
import jax
import jax.numpy as jnp
from jax import lax
from jax.sharding import PartitionSpec as P

MOST = 32


contract_rows = (((0,), (0,)), ((), ()))
contract_cols = (((1,), (1,)), ((), ()))


def silu_parts(pre_gate):
    sigmoid_gate = jax.nn.sigmoid(pre_gate)
    return (pre_gate * sigmoid_gate, sigmoid_gate * (1.0 + pre_gate * (1.0 - sigmoid_gate)))


def local_grads(pre_gate, pre_up, grad_act):
    active, slope_gate = silu_parts(pre_gate)
    hidden = (active * pre_up).astype(jnp.bfloat16)
    grad_gate = (grad_act * pre_up * slope_gate).astype(jnp.bfloat16)
    grad_up = (grad_act * active).astype(jnp.bfloat16)
    return (hidden, grad_gate, grad_up)


def shards(tokens, out_grad, expert_ids, gate_probs, w_gate, w_up, w_down):
    tok_rows, slab_width = tokens.shape
    owners = lax.axis_size("expert")
    experts = owners * w_gate.shape[0]
    pick_ids = expert_ids.T.reshape(-1)
    onehot = (pick_ids[:, None] == jnp.arange(experts, dtype=jnp.int32)[None, :]).astype(jnp.int32)
    rank_in = jnp.sum((jnp.cumsum(onehot, axis=0) - 1) * onehot, axis=1)
    slot_of = pick_ids * MOST + rank_in
    placing = (jnp.arange(experts * MOST, dtype=jnp.int32)[:, None] == slot_of[None, :]).astype(
        jnp.bfloat16
    )
    row_pick = jnp.concatenate([tokens, tokens], axis=0)
    grad_pick = jnp.concatenate([out_grad, out_grad], axis=0)
    scaled = (gate_probs.T.reshape(-1)[:, None] * grad_pick.astype(jnp.float32)).astype(
        jnp.bfloat16
    )
    both = jnp.concatenate([row_pick, scaled], axis=1)
    send = (
        jnp.dot(placing, both, preferred_element_type=jnp.float32)
        .astype(jnp.bfloat16)
        .reshape(experts, MOST, 2 * slab_width)
    )
    arrived = lax.all_to_all(send, "expert", split_axis=0, concat_axis=0, tiled=True)
    arrived_tokens = arrived[:, :, :slab_width]
    arrived_grads = arrived[:, :, slab_width:]
    flat_tokens = arrived_tokens.reshape(-1, slab_width)
    flat_grads = arrived_grads.reshape(-1, slab_width)
    gate_mat = w_gate[0]
    up_mat = w_up[0]
    down_mat = w_down[0]
    hidden_width = gate_mat.shape[1]
    gate_up_mat = jnp.concatenate([gate_mat, up_mat], axis=1)
    part_gate_up = jnp.dot(flat_tokens, gate_up_mat, preferred_element_type=jnp.float32)
    part_act = lax.dot_general(
        flat_grads, down_mat, contract_cols, preferred_element_type=jnp.float32
    )
    summed_gate_up, summed_act = lax.psum(
        (part_gate_up.astype(jnp.bfloat16), part_act.astype(jnp.bfloat16)), "dp"
    )
    wide = summed_gate_up.astype(jnp.float32)
    pre_gate = wide[:, :hidden_width]
    pre_up = wide[:, hidden_width:]
    grad_act = summed_act.astype(jnp.float32)
    hidden, grad_gate, grad_up = local_grads(pre_gate, pre_up, grad_act)
    grad_gate, grad_up = lax.optimization_barrier((grad_gate, grad_up))
    slot_grad = lax.dot_general(
        jnp.concatenate([grad_gate, grad_up], axis=1),
        gate_up_mat,
        contract_cols,
        preferred_element_type=jnp.float32,
    )
    gate_grads = lax.dot_general(
        flat_tokens, grad_gate, contract_rows, preferred_element_type=jnp.float32
    )[None]
    up_grads = lax.dot_general(
        flat_tokens, grad_up, contract_rows, preferred_element_type=jnp.float32
    )[None]
    down_grads = lax.dot_general(
        hidden, flat_grads, contract_rows, preferred_element_type=jnp.float32
    )[None]
    returned = lax.all_to_all(
        slot_grad.reshape(experts, MOST, slab_width).astype(jnp.bfloat16),
        "expert",
        split_axis=0,
        concat_axis=0,
        tiled=True,
    )
    flat_back = returned.reshape(experts * MOST, slab_width)
    per_pick = lax.dot_general(placing, flat_back, contract_rows, preferred_element_type=jnp.float32)
    token_grad = (per_pick[:tok_rows] + per_pick[tok_rows:]).astype(jnp.bfloat16)
    return (token_grad, gate_grads, up_grads, down_grads)


def solution(mesh):
    in_specs = (
        P("expert", "dp"),
        P("expert", "dp"),
        P("expert", None),
        P("expert", None),
        P("expert", "dp", None),
        P("expert", "dp", None),
        P("expert", None, "dp"),
    )
    out_specs = (
        P("expert", "dp"),
        P("expert", "dp", None),
        P("expert", "dp", None),
        P("expert", None, "dp"),
    )
    return jax.shard_map(shards, mesh=mesh, in_specs=in_specs, out_specs=out_specs, check_vma=False)
```

```python
import jax
import jax.numpy as jnp
from jax import lax
from jax.sharding import PartitionSpec as P

MOST = 32


contract_rows = (((0,), (0,)), ((), ()))
contract_cols = (((1,), (1,)), ((), ()))


def silu_parts(pre_gate):
    sigmoid_gate = jax.nn.sigmoid(pre_gate)
    return (pre_gate * sigmoid_gate, sigmoid_gate * (1.0 + pre_gate * (1.0 - sigmoid_gate)))


def local_grads(pre_gate, pre_up, grad_act):
    active, slope_gate = silu_parts(pre_gate)
    hidden = (active * pre_up).astype(jnp.bfloat16)
    grad_gate = (grad_act * pre_up * slope_gate).astype(jnp.bfloat16)
    grad_up = (grad_act * active).astype(jnp.bfloat16)
    return (hidden, grad_gate, grad_up)


def shards(tokens, out_grad, expert_ids, gate_probs, w_gate, w_up, w_down):
    tok_rows, slab_width = tokens.shape
    owners = lax.axis_size("expert")
    experts = owners * w_gate.shape[0]
    pick_ids = expert_ids.T.reshape(-1)
    onehot = (pick_ids[:, None] == jnp.arange(experts, dtype=jnp.int32)[None, :]).astype(jnp.bfloat16)
    picks = pick_ids.shape[0]
    order = jnp.arange(picks, dtype=jnp.int32)
    earlier = (order[None, :] < order[:, None]).astype(jnp.bfloat16)
    before = jnp.dot(earlier, onehot, preferred_element_type=jnp.float32)
    rank_in = jnp.sum(before * onehot.astype(jnp.float32), axis=1).astype(jnp.int32)
    slot_of = pick_ids * MOST + rank_in
    placing = (jnp.arange(experts * MOST, dtype=jnp.int32)[:, None] == slot_of[None, :]).astype(
        jnp.bfloat16
    )
    row_pick = jnp.concatenate([tokens, tokens], axis=0)
    grad_pick = jnp.concatenate([out_grad, out_grad], axis=0)
    scaled = (gate_probs.T.reshape(-1)[:, None] * grad_pick.astype(jnp.float32)).astype(
        jnp.bfloat16
    )
    both = jnp.concatenate([row_pick, scaled], axis=1)
    send = (
        jnp.dot(placing, both, preferred_element_type=jnp.float32)
        .astype(jnp.bfloat16)
        .reshape(experts, MOST, 2 * slab_width)
    )
    arrived = lax.all_to_all(send, "expert", split_axis=0, concat_axis=0, tiled=True)
    arrived_tokens = arrived[:, :, :slab_width]
    arrived_grads = arrived[:, :, slab_width:]
    flat_tokens = arrived_tokens.reshape(-1, slab_width)
    flat_grads = arrived_grads.reshape(-1, slab_width)
    gate_mat = w_gate[0]
    up_mat = w_up[0]
    down_mat = w_down[0]
    part_gate = jnp.dot(flat_tokens, gate_mat, preferred_element_type=jnp.float32)
    part_up = jnp.dot(flat_tokens, up_mat, preferred_element_type=jnp.float32)
    part_act = lax.dot_general(
        flat_grads, down_mat, contract_cols, preferred_element_type=jnp.float32
    )
    pre_gate, pre_up, grad_act = (
        lax.psum(part_gate.astype(jnp.bfloat16), "dp").astype(jnp.float32),
        lax.psum(part_up.astype(jnp.bfloat16), "dp").astype(jnp.float32),
        lax.psum(part_act.astype(jnp.bfloat16), "dp").astype(jnp.float32),
    )
    hidden, grad_gate, grad_up = local_grads(pre_gate, pre_up, grad_act)
    grad_gate, grad_up = lax.optimization_barrier((grad_gate, grad_up))
    slot_grad = lax.dot_general(
        grad_gate, gate_mat, contract_cols, preferred_element_type=jnp.float32
    )
    slot_grad = slot_grad + lax.dot_general(
        grad_up, up_mat, contract_cols, preferred_element_type=jnp.float32
    )
    gate_grads = lax.dot_general(
        flat_tokens, grad_gate, contract_rows, preferred_element_type=jnp.float32
    )[None]
    up_grads = lax.dot_general(
        flat_tokens, grad_up, contract_rows, preferred_element_type=jnp.float32
    )[None]
    down_grads = lax.dot_general(
        hidden, flat_grads, contract_rows, preferred_element_type=jnp.float32
    )[None]
    returned = lax.all_to_all(
        slot_grad.reshape(experts, MOST, slab_width).astype(jnp.bfloat16),
        "expert",
        split_axis=0,
        concat_axis=0,
        tiled=True,
    )
    flat_back = returned.reshape(experts * MOST, slab_width)
    per_pick = lax.dot_general(placing, flat_back, contract_rows, preferred_element_type=jnp.float32)
    token_grad = (per_pick[:tok_rows] + per_pick[tok_rows:]).astype(jnp.bfloat16)
    return (token_grad, gate_grads, up_grads, down_grads)


def solution(mesh):
    in_specs = (
        P("expert", "dp"),
        P("expert", "dp"),
        P("expert", None),
        P("expert", None),
        P("expert", "dp", None),
        P("expert", "dp", None),
        P("expert", None, "dp"),
    )
    out_specs = (
        P("expert", "dp"),
        P("expert", "dp", None),
        P("expert", "dp", None),
        P("expert", None, "dp"),
    )
    return jax.shard_map(shards, mesh=mesh, in_specs=in_specs, out_specs=out_specs, check_vma=False)
```
